128 devices in a mesh: section: 2 (over core), seq: 4 (over x), tensor: 16 (over z, y).
Axes of the slice: x: 4, y: 4, z: 4, core: 2. Of those that a mesh axis runs over, the one named last changes fastest.
Arguments:
- queries: bfloat16 [2560, 8192], P(('section', 'seq'), 'tensor'), may hold values from -200 to 200
- neighbours: bfloat16 [10240, 8192], P(('section', 'seq', 'tensor')), may hold values from -6 to 6
- kv_weight: bfloat16 [2, 8192, 8192], P(None, None, 'tensor'), may hold values from -0.0625 to 0.0625
- out_weight: bfloat16 [8192, 8192], P('tensor'), may hold values from -0.5 to 0.5
- slot_map: int32 [40], replicated, may hold values from 0 to 39, as said below
Outputs:
- mixed: bfloat16 [2560, 8192], P(('section', 'seq', 'tensor'))
The draws below stay inside these ranges and needn't reach their ends.
Inputs may be any that keep to these rules, and one draw needn't show every extreme that they name: `slot_map`: distinct numbers; slot s lies on encoder shard s // 5; at most 2 spans of one sequence shard map to one encoder shard, and that many do for some pair of shards.
All inputs are finite; a program needn't handle non-finite values.
Results may differ from the reference program's by a relative error of at most 0.013.
Values may be sent and summed in bfloat16 or wider, within the bound.
No kernel may reach another device: no remote copies, remote signals or barrier semaphores. Data moves between devices by JAX's collectives and lax.ppermute only.
A program may use at most 128 MiB of HBM per device.

```python
import math
import jax
import jax.numpy as jnp
from jax import lax

D = 8192
HEADS = 64
HD = 128
SPAN = 64
PEER = 2
CH_DEV = 5
CAPC = 5
KEYS = 256
GROUPS = 8
NCH = 40
SEQ = 2560


def draw_slot_map(key, part):
    key_seq = jax.random.fold_in(key, 11)
    key_enc = jax.random.fold_in(key, 12)
    key_order = jax.random.fold_in(key, 13)
    key_slots = jax.random.fold_in(key, 14)
    seq_perm = jax.random.permutation(key_seq, GROUPS).astype(jnp.int32)
    enc_perm = jax.random.permutation(key_enc, GROUPS).astype(jnp.int32)
    span_ids = jnp.arange(NCH, dtype=jnp.int32)
    shard = span_ids // CH_DEV
    order_score = jax.random.permutation(key_order, NCH).astype(jnp.int32)
    same_shard = shard[:, None] == shard[None, :]
    lower = order_score[None, :] < order_score[:, None]
    position = jnp.sum((same_shard & lower).astype(jnp.int32), axis=1).astype(jnp.int32)
    offset = position // PEER
    encoder = enc_perm[(seq_perm[shard] + offset) % GROUPS]
    slot_score = jax.random.permutation(key_slots, NCH).astype(jnp.int32)
    same_enc = encoder[:, None] == encoder[None, :]
    lower_slot = slot_score[None, :] < slot_score[:, None]
    rank = jnp.sum((same_enc & lower_slot).astype(jnp.int32), axis=1).astype(jnp.int32)
    return (encoder * CAPC + rank).astype(jnp.int32)


def draw_queries(key, part):
    key_main = jax.random.fold_in(key, 21)
    values = jnp.clip(jax.random.normal(key_main, (SEQ, D), jnp.float32), -6.0, 6.0)
    return values.astype(jnp.bfloat16)


def block_scale(own_key, shape, pieces, low, largest):
    level, own = 1.0, jax.random.fold_in(own_key, 6)
    for dim, blocks in pieces:
        draws = jnp.exp(jax.random.uniform(jax.random.fold_in(own, dim), (blocks,), jnp.float32, low / len(pieces), largest / len(pieces)))
        level = level * jnp.repeat(draws, shape[dim] // blocks).reshape([-1 if axis == dim else 1 for axis in range(len(shape))])
    return level


def scatter_about(own_key, dims, width, most, split=(), kind=jnp.bfloat16):
    result = jax.random.normal(own_key, dims, jnp.float32) * width
    if len(split) > 0:
        result = block_scale(own_key, dims, split, -0.22, 0.18) * result
    return jnp.clip(result, min=-most, max=most).astype(kind)


def setup_inputs(seed: int = 0) -> dict:
    key_of = jax.random.split(jax.random.key(seed), 6)
    return {
        "queries": draw_queries(jax.random.fold_in(key_of[5], 71), 0),
        "neighbours": scatter_about(key_of[1], (GROUPS * CAPC * KEYS, D), 1.0, 6.0, ((0, 128),)),
        "kv_weight": scatter_about(key_of[2], (2, D, D), D ** -0.5, 0.0625, ((2, 16),)),
        "out_weight": scatter_about(key_of[3], (D, D), HD ** -0.5, 0.5, ((0, 16),)),
        "slot_map": draw_slot_map(jax.random.fold_in(key_of[5], 71), 0),
    }


def reference(queries, neighbours, kv_weight, out_weight, slot_map):
    span_rows = neighbours.reshape(GROUPS * CAPC, KEYS, D)[slot_map].reshape(NCH * KEYS, D)
    keys = jnp.dot(span_rows, kv_weight[0], preferred_element_type=jnp.float32).astype(jnp.bfloat16)
    values = jnp.dot(span_rows, kv_weight[1], preferred_element_type=jnp.float32).astype(jnp.bfloat16)
    keys = keys.reshape(NCH, KEYS, HEADS, HD).astype(jnp.float32)
    values = values.reshape(NCH, KEYS, HEADS, HD).astype(jnp.float32)
    query_heads = queries.reshape(NCH, SPAN, HEADS, HD).astype(jnp.float32)
    scores = jnp.einsum('cqhd,ckhd->chqk', query_heads, keys) * (1.0 / math.sqrt(HD))
    peak = lax.optimization_barrier(jnp.max(scores, axis=-1, keepdims=True))
    expo = jnp.exp(scores - peak)
    weights = (expo / lax.optimization_barrier(jnp.sum(expo, axis=-1, keepdims=True))).astype(jnp.bfloat16)
    attended = jnp.einsum('chqk,ckhd->cqhd', weights.astype(jnp.float32), values)
    attended = attended.astype(jnp.bfloat16).reshape(SEQ, D)
    return jnp.dot(attended, out_weight, preferred_element_type=jnp.float32).astype(jnp.bfloat16)
```

```python
import math

import jax
import jax.numpy as jnp
from jax import lax
from jax.sharding import PartitionSpec as P

HD = 128
SPAN = 64
PEER = 2
CH_DEV = 5
CAPC = 5
KEYS = 256
ROW_CHUNKS = 5


def attend(query_block, keys, values):
    scores = jnp.einsum(
        "bqhd,bkhd->bhqk", query_block, keys, preferred_element_type=jnp.float32
    )
    scores = scores * (1.0 / math.sqrt(HD))
    peak = jnp.max(scores, axis=-1, keepdims=True)
    expo = jnp.exp(scores - peak)
    weights = (expo / jnp.sum(expo, axis=-1, keepdims=True)).astype(jnp.bfloat16)
    result = jnp.einsum(
        "bhqk,bkhd->bqhd", weights, values, preferred_element_type=jnp.float32
    )
    return result.astype(jnp.bfloat16)


def on_device(queries, neighbours, kv_weight, out_weight, slot_map):
    groups = lax.axis_size(("section", "seq"))
    group_index = lax.axis_index(("section", "seq"))
    tensor_size = lax.axis_size("tensor")
    cols = kv_weight.shape[2]
    heads_local = cols // HD
    spans = slot_map.shape[0]
    rows_local = neighbours.shape[0]

    span_ids = jnp.arange(spans, dtype=jnp.int32)
    owner_shard = slot_map // CAPC
    slot_index = slot_map % CAPC
    seq_owner = span_ids // CH_DEV
    earlier = (seq_owner[:, None] == seq_owner[None, :]) & (
        owner_shard[:, None] == owner_shard[None, :]
    )
    earlier = earlier & (span_ids[None, :] < span_ids[:, None])
    arrival = jnp.sum(earlier.astype(jnp.int32), axis=1)

    peer_ids = jnp.arange(groups, dtype=jnp.int32)[:, None, None]
    place_ids = jnp.arange(PEER, dtype=jnp.int32)[None, :, None]

    own_spans = group_index * CH_DEV + jnp.arange(CH_DEV, dtype=jnp.int32)
    own_owner = owner_shard[own_spans]
    own_arrival = arrival[own_spans]
    pick_q = (own_owner[None, None, :] == peer_ids) & (own_arrival[None, None, :] == place_ids)
    send_q_idx = jnp.sum(
        jnp.where(pick_q, jnp.arange(CH_DEV, dtype=jnp.int32)[None, None, :], 0), axis=-1
    )
    query_blocks = queries.reshape(CH_DEV, SPAN, cols)
    send_q = query_blocks[send_q_idx]
    recv_q = lax.all_to_all(send_q, ("section", "seq"), split_axis=0, concat_axis=0, tiled=True)

    my_slots = group_index * CAPC + jnp.arange(CAPC, dtype=jnp.int32)
    hit = slot_map[None, :] == my_slots[:, None]
    slot_span = jnp.sum(jnp.where(hit, span_ids[None, :], 0), axis=1)
    slot_group = slot_span // CH_DEV
    slot_place = arrival[slot_span]
    q_for_slot = recv_q[slot_group, slot_place].reshape(CAPC, SPAN, heads_local, HD)

    sub = rows_local // ROW_CHUNKS
    nb_chunks = neighbours.reshape(ROW_CHUNKS, sub, neighbours.shape[1])
    kv_parts = []
    for i in range(ROW_CHUNKS):
        rows = lax.all_gather(nb_chunks[i], "tensor", axis=0, tiled=True)
        part = jnp.einsum("rd,kde->rke", rows, kv_weight, preferred_element_type=jnp.float32)
        kv_parts.append(part.astype(jnp.bfloat16).reshape(tensor_size, sub, 2, cols))
    kv = jnp.stack(kv_parts, axis=1).reshape(tensor_size * rows_local, 2, cols)
    kv = kv.reshape(CAPC, KEYS, 2, heads_local, HD)
    attended = attend(q_for_slot, kv[:, :, 0], kv[:, :, 1]).reshape(CAPC, SPAN, cols)

    pick_a = (slot_group[None, None, :] == peer_ids) & (slot_place[None, None, :] == place_ids)
    send_a_idx = jnp.sum(
        jnp.where(pick_a, jnp.arange(CAPC, dtype=jnp.int32)[None, None, :], 0), axis=-1
    )
    send_a = attended[send_a_idx]
    recv_a = lax.all_to_all(send_a, ("section", "seq"), split_axis=0, concat_axis=0, tiled=True)
    attended_flat = recv_a[own_owner, own_arrival].reshape(CH_DEV * SPAN, cols)

    partial = jnp.dot(attended_flat, out_weight, preferred_element_type=jnp.float32)
    partial = partial.astype(jnp.bfloat16).reshape(tensor_size, -1, out_weight.shape[1])
    mixed = lax.psum_scatter(partial, "tensor", scatter_dimension=0, tiled=True)
    return mixed.reshape(-1, out_weight.shape[1])


def solution(mesh):
    placed = (
        P(("section", "seq"), "tensor"),
        P(("section", "seq", "tensor"), None),
        P(None, None, "tensor"),
        P("tensor", None),
        P(),
    )
    return jax.shard_map(
        on_device,
        mesh=mesh,
        in_specs=placed,
        out_specs=P(("section", "seq", "tensor"), None),
        check_vma=False,
    )
```

```python
import math

import jax
import jax.numpy as jnp
from jax import lax
from jax.sharding import PartitionSpec as P

HD = 128
SPAN = 64
PEER = 2
CH_DEV = 5
CAPC = 5
KEYS = 256
ROW_CHUNKS = 1


def attend(query_block, keys, values):
    scores = jnp.einsum(
        "bqhd,bkhd->bhqk", query_block, keys, preferred_element_type=jnp.float32
    )
    scores = scores * (1.0 / math.sqrt(HD))
    peak = jnp.max(scores, axis=-1, keepdims=True)
    expo = jnp.exp(scores - peak)
    weights = (expo / jnp.sum(expo, axis=-1, keepdims=True)).astype(jnp.bfloat16)
    result = jnp.einsum(
        "bhqk,bkhd->bqhd", weights, values, preferred_element_type=jnp.float32
    )
    return result.astype(jnp.bfloat16)


def on_device(queries, neighbours, kv_weight, out_weight, slot_map):
    groups = lax.axis_size(("section", "seq"))
    group_index = lax.axis_index(("section", "seq"))
    tensor_size = lax.axis_size("tensor")
    cols = kv_weight.shape[2]
    heads_local = cols // HD
    spans = slot_map.shape[0]
    rows_local = neighbours.shape[0]

    span_ids = jnp.arange(spans, dtype=jnp.int32)
    owner_shard = slot_map // CAPC
    slot_index = slot_map % CAPC
    seq_owner = span_ids // CH_DEV
    earlier = (seq_owner[:, None] == seq_owner[None, :]) & (
        owner_shard[:, None] == owner_shard[None, :]
    )
    earlier = earlier & (span_ids[None, :] < span_ids[:, None])
    arrival = jnp.sum(earlier.astype(jnp.int32), axis=1)

    peer_ids = jnp.arange(groups, dtype=jnp.int32)[:, None, None]
    place_ids = jnp.arange(PEER, dtype=jnp.int32)[None, :, None]

    own_spans = group_index * CH_DEV + jnp.arange(CH_DEV, dtype=jnp.int32)
    own_owner = owner_shard[own_spans]
    own_arrival = arrival[own_spans]
    pick_q = (own_owner[None, None, :] == peer_ids) & (own_arrival[None, None, :] == place_ids)
    send_q_idx = jnp.sum(
        jnp.where(pick_q, jnp.arange(CH_DEV, dtype=jnp.int32)[None, None, :], 0), axis=-1
    )
    query_blocks = queries.reshape(CH_DEV, SPAN, cols)
    send_q = query_blocks[send_q_idx]
    recv_q = lax.all_to_all(send_q, ("section", "seq"), split_axis=0, concat_axis=0, tiled=True)

    my_slots = group_index * CAPC + jnp.arange(CAPC, dtype=jnp.int32)
    hit = slot_map[None, :] == my_slots[:, None]
    slot_span = jnp.sum(jnp.where(hit, span_ids[None, :], 0), axis=1)
    slot_group = slot_span // CH_DEV
    slot_place = arrival[slot_span]
    q_for_slot = recv_q[slot_group, slot_place].reshape(CAPC, SPAN, heads_local, HD)

    sub = rows_local // ROW_CHUNKS
    nb_chunks = neighbours.reshape(ROW_CHUNKS, sub, neighbours.shape[1])
    kv_parts = []
    for i in range(ROW_CHUNKS):
        rows = lax.all_gather(nb_chunks[i], "tensor", axis=0, tiled=True)
        part = jnp.einsum("rd,kde->rke", rows, kv_weight, preferred_element_type=jnp.float32)
        kv_parts.append(part.astype(jnp.bfloat16).reshape(tensor_size, sub, 2, cols))
    kv = jnp.stack(kv_parts, axis=1).reshape(tensor_size * rows_local, 2, cols)
    kv = kv.reshape(CAPC, KEYS, 2, heads_local, HD)
    attended = attend(q_for_slot, kv[:, :, 0], kv[:, :, 1]).reshape(CAPC, SPAN, cols)

    pick_a = (slot_group[None, None, :] == peer_ids) & (slot_place[None, None, :] == place_ids)
    send_a_idx = jnp.sum(
        jnp.where(pick_a, jnp.arange(CAPC, dtype=jnp.int32)[None, None, :], 0), axis=-1
    )
    send_a = attended[send_a_idx]
    recv_a = lax.all_to_all(send_a, ("section", "seq"), split_axis=0, concat_axis=0, tiled=True)
    attended_flat = recv_a[own_owner, own_arrival].reshape(CH_DEV * SPAN, cols)

    partial = jnp.dot(attended_flat, out_weight, preferred_element_type=jnp.float32)
    partial = partial.astype(jnp.bfloat16).reshape(tensor_size, -1, out_weight.shape[1])
    mixed = lax.psum_scatter(partial, "tensor", scatter_dimension=0, tiled=True)
    return mixed.reshape(-1, out_weight.shape[1])


def solution(mesh):
    placed = (
        P(("section", "seq"), "tensor"),
        P(("section", "seq", "tensor"), None),
        P(None, None, "tensor"),
        P("tensor", None),
        P(),
    )
    return jax.shard_map(
        on_device,
        mesh=mesh,
        in_specs=placed,
        out_specs=P(("section", "seq", "tensor"), None),
        check_vma=False,
    )
```

```python
import math

import jax
import jax.numpy as jnp
from jax import lax
from jax.sharding import PartitionSpec as P

HD = 128
SPAN = 64
PEER = 2
CH_DEV = 5
CAPC = 5
KEYS = 256
ROW_CHUNKS = 1


def attend(query_block, keys, values):
    scores = jnp.einsum(
        "bqhd,bkhd->bhqk", query_block, keys, preferred_element_type=jnp.float32
    )
    scores = scores * (1.0 / math.sqrt(HD))
    peak = jnp.max(scores, axis=-1, keepdims=True)
    expo = jnp.exp(scores - peak)
    weights = (expo / jnp.sum(expo, axis=-1, keepdims=True)).astype(jnp.bfloat16)
    result = jnp.einsum(
        "bhqk,bkhd->bqhd", weights, values, preferred_element_type=jnp.float32
    )
    return result.astype(jnp.bfloat16)


def on_device(queries, neighbours, kv_weight, out_weight, slot_map):
    groups = lax.axis_size(("section", "seq"))
    group_index = lax.axis_index(("section", "seq"))
    tensor_size = lax.axis_size("tensor")
    cols = kv_weight.shape[2]
    heads_local = cols // HD
    spans = slot_map.shape[0]
    rows_local = neighbours.shape[0]

    span_ids = jnp.arange(spans, dtype=jnp.int32)
    owner_shard = slot_map // CAPC
    slot_index = slot_map % CAPC
    seq_owner = span_ids // CH_DEV
    earlier = (seq_owner[:, None] == seq_owner[None, :]) & (
        owner_shard[:, None] == owner_shard[None, :]
    )
    earlier = earlier & (span_ids[None, :] < span_ids[:, None])
    arrival = jnp.sum(earlier.astype(jnp.int32), axis=1)

    peer_ids = jnp.arange(groups, dtype=jnp.int32)[:, None, None]
    place_ids = jnp.arange(PEER, dtype=jnp.int32)[None, :, None]

    own_spans = group_index * CH_DEV + jnp.arange(CH_DEV, dtype=jnp.int32)
    own_owner = owner_shard[own_spans]
    own_arrival = arrival[own_spans]
    pick_q = (own_owner[None, None, :] == peer_ids) & (own_arrival[None, None, :] == place_ids)
    send_q_idx = jnp.sum(
        jnp.where(pick_q, jnp.arange(CH_DEV, dtype=jnp.int32)[None, None, :], 0), axis=-1
    )
    query_blocks = queries.reshape(CH_DEV, SPAN, cols)
    send_q = query_blocks[send_q_idx]
    recv_q = lax.all_to_all(send_q, ("section", "seq"), split_axis=0, concat_axis=0, tiled=True)

    my_slots = group_index * CAPC + jnp.arange(CAPC, dtype=jnp.int32)
    hit = slot_map[None, :] == my_slots[:, None]
    slot_span = jnp.sum(jnp.where(hit, span_ids[None, :], 0), axis=1)
    slot_group = slot_span // CH_DEV
    slot_place = arrival[slot_span]
    q_for_slot = recv_q[slot_group, slot_place].reshape(CAPC, SPAN, heads_local, HD)

    sub = rows_local // ROW_CHUNKS
    nb_chunks = neighbours.reshape(ROW_CHUNKS, sub, neighbours.shape[1])
    kv_parts = []
    for i in range(ROW_CHUNKS):
        rows = lax.all_gather(nb_chunks[i], "tensor", axis=0, tiled=True)
        part = jnp.einsum("rd,kde->rke", rows, kv_weight, preferred_element_type=jnp.float32)
        kv_parts.append(part.astype(jnp.bfloat16).reshape(tensor_size, sub, 2, cols))
    kv = jnp.stack(kv_parts, axis=1).reshape(tensor_size * rows_local, 2, cols)
    kv = kv.reshape(CAPC, KEYS, 2, heads_local, HD)
    attended = attend(q_for_slot, kv[:, :, 0], kv[:, :, 1]).reshape(CAPC, SPAN, cols)

    pick_a = (slot_group[None, None, :] == peer_ids) & (slot_place[None, None, :] == place_ids)
    send_a_idx = jnp.sum(
        jnp.where(pick_a, jnp.arange(CAPC, dtype=jnp.int32)[None, None, :], 0), axis=-1
    )
    send_a = attended[send_a_idx]
    recv_a = lax.all_to_all(send_a, ("section", "seq"), split_axis=0, concat_axis=0, tiled=True)
    attended_rows = recv_a[own_owner, own_arrival].reshape(tensor_size, -1, cols)

    partial = jnp.einsum(
        "srk,kn->srn", attended_rows, out_weight, preferred_element_type=jnp.float32
    ).astype(jnp.bfloat16)
    mixed = lax.psum_scatter(partial, "tensor", scatter_dimension=0, tiled=True)
    return mixed.reshape(-1, out_weight.shape[1])


def solution(mesh):
    placed = (
        P(("section", "seq"), "tensor"),
        P(("section", "seq", "tensor"), None),
        P(None, None, "tensor"),
        P("tensor", None),
        P(),
    )
    return jax.shard_map(
        on_device,
        mesh=mesh,
        in_specs=placed,
        out_specs=P(("section", "seq", "tensor"), None),
        check_vma=False,
    )
```

```python
import math

import jax
import jax.numpy as jnp
from jax import lax
from jax.sharding import PartitionSpec as P

HD = 128
SPAN = 64
PEER = 2
CH_DEV = 5
CAPC = 5
KEYS = 256


def attend(query_block, keys, values):
    scores = jnp.einsum(
        "bqhd,bkhd->bhqk", query_block, keys, preferred_element_type=jnp.float32
    )
    scores = scores * (1.0 / math.sqrt(HD))
    peak = jnp.max(scores, axis=-1, keepdims=True)
    expo = jnp.exp(scores - peak)
    weights = (expo / jnp.sum(expo, axis=-1, keepdims=True)).astype(jnp.bfloat16)
    result = jnp.einsum(
        "bhqk,bkhd->bqhd", weights, values, preferred_element_type=jnp.float32
    )
    return result.astype(jnp.bfloat16)


def on_device(queries, neighbours, kv_weight, out_weight, slot_map):
    groups = lax.axis_size(("section", "seq"))
    group_index = lax.axis_index(("section", "seq"))
    tensor_size = lax.axis_size("tensor")
    cols = kv_weight.shape[2]
    heads_local = cols // HD
    spans = slot_map.shape[0]
    rows_local = neighbours.shape[0]

    span_ids = jnp.arange(spans, dtype=jnp.int32)
    owner_shard = slot_map // CAPC
    slot_index = slot_map % CAPC
    seq_owner = span_ids // CH_DEV
    earlier = (seq_owner[:, None] == seq_owner[None, :]) & (
        owner_shard[:, None] == owner_shard[None, :]
    )
    earlier = earlier & (span_ids[None, :] < span_ids[:, None])
    arrival = jnp.sum(earlier.astype(jnp.int32), axis=1)

    peer_ids = jnp.arange(groups, dtype=jnp.int32)[:, None, None]
    place_ids = jnp.arange(PEER, dtype=jnp.int32)[None, :, None]

    own_spans = group_index * CH_DEV + jnp.arange(CH_DEV, dtype=jnp.int32)
    own_owner = owner_shard[own_spans]
    own_arrival = arrival[own_spans]
    pick_q = (own_owner[None, None, :] == peer_ids) & (own_arrival[None, None, :] == place_ids)
    send_q_idx = jnp.sum(
        jnp.where(pick_q, jnp.arange(CH_DEV, dtype=jnp.int32)[None, None, :], 0), axis=-1
    )
    query_blocks = queries.reshape(CH_DEV, SPAN, cols)
    send_q = query_blocks[send_q_idx]
    recv_q = lax.all_to_all(send_q, ("section", "seq"), split_axis=0, concat_axis=0, tiled=True)

    my_slots = group_index * CAPC + jnp.arange(CAPC, dtype=jnp.int32)
    hit = slot_map[None, :] == my_slots[:, None]
    slot_span = jnp.sum(jnp.where(hit, span_ids[None, :], 0), axis=1)
    slot_group = slot_span // CH_DEV
    slot_place = arrival[slot_span]
    q_for_slot = recv_q[slot_group, slot_place].reshape(CAPC, SPAN, heads_local, HD)

    rows = lax.all_gather(neighbours, "tensor", axis=0, tiled=True)
    rows = rows.reshape(CAPC, KEYS, rows.shape[1])
    keys = jnp.einsum("skd,de->ske", rows, kv_weight[0], preferred_element_type=jnp.float32)
    values = jnp.einsum("skd,de->ske", rows, kv_weight[1], preferred_element_type=jnp.float32)
    keys = keys.astype(jnp.bfloat16).reshape(CAPC, KEYS, heads_local, HD)
    values = values.astype(jnp.bfloat16).reshape(CAPC, KEYS, heads_local, HD)
    attended = attend(q_for_slot, keys, values).reshape(CAPC, SPAN, cols)

    pick_a = (slot_group[None, None, :] == peer_ids) & (slot_place[None, None, :] == place_ids)
    send_a_idx = jnp.sum(
        jnp.where(pick_a, jnp.arange(CAPC, dtype=jnp.int32)[None, None, :], 0), axis=-1
    )
    send_a = attended[send_a_idx]
    recv_a = lax.all_to_all(send_a, ("section", "seq"), split_axis=0, concat_axis=0, tiled=True)
    attended_rows = recv_a[own_owner, own_arrival].reshape(tensor_size, -1, cols)

    partial = jnp.einsum(
        "srk,kn->srn", attended_rows, out_weight, preferred_element_type=jnp.float32
    ).astype(jnp.bfloat16)
    mixed = lax.psum_scatter(partial, "tensor", scatter_dimension=0, tiled=True)
    return mixed.reshape(-1, out_weight.shape[1])


def solution(mesh):
    placed = (
        P(("section", "seq"), "tensor"),
        P(("section", "seq", "tensor"), None),
        P(None, None, "tensor"),
        P("tensor", None),
        P(),
    )
    return jax.shard_map(
        on_device,
        mesh=mesh,
        in_specs=placed,
        out_specs=P(("section", "seq", "tensor"), None),
        check_vma=False,
    )
```

```python
import math

import jax
import jax.numpy as jnp
from jax import lax
from jax.sharding import PartitionSpec as P

HD = 128
SPAN = 64
PEER = 2
CH_DEV = 5
CAPC = 5
KEYS = 256


def attend(query_block, keys, values):
    scores = jnp.einsum(
        "bqhd,bkhd->bhqk", query_block, keys, preferred_element_type=jnp.float32
    )
    scores = scores * (1.0 / math.sqrt(HD))
    peak = jnp.max(scores, axis=-1, keepdims=True)
    expo = jnp.exp(scores - peak)
    weights = (expo / jnp.sum(expo, axis=-1, keepdims=True)).astype(jnp.bfloat16)
    result = jnp.einsum(
        "bhqk,bkhd->bqhd", weights, values, preferred_element_type=jnp.float32
    )
    return result.astype(jnp.bfloat16)


def on_device(queries, neighbours, kv_weight, out_weight, slot_map):
    groups = lax.axis_size(("section", "seq"))
    group_index = lax.axis_index(("section", "seq"))
    tensor_size = lax.axis_size("tensor")
    cols = kv_weight.shape[2]
    heads_local = cols // HD
    spans = slot_map.shape[0]
    rows_local = neighbours.shape[0]

    span_ids = jnp.arange(spans, dtype=jnp.int32)
    owner_shard = slot_map // CAPC
    slot_index = slot_map % CAPC
    seq_owner = span_ids // CH_DEV
    earlier = (seq_owner[:, None] == seq_owner[None, :]) & (
        owner_shard[:, None] == owner_shard[None, :]
    )
    earlier = earlier & (span_ids[None, :] < span_ids[:, None])
    arrival = jnp.sum(earlier.astype(jnp.int32), axis=1)

    peer_ids = jnp.arange(groups, dtype=jnp.int32)[:, None, None]
    place_ids = jnp.arange(PEER, dtype=jnp.int32)[None, :, None]

    own_spans = group_index * CH_DEV + jnp.arange(CH_DEV, dtype=jnp.int32)
    own_owner = owner_shard[own_spans]
    own_arrival = arrival[own_spans]
    pick_q = (own_owner[None, None, :] == peer_ids) & (own_arrival[None, None, :] == place_ids)
    send_q_idx = jnp.sum(
        jnp.where(pick_q, jnp.arange(CH_DEV, dtype=jnp.int32)[None, None, :], 0), axis=-1
    )
    query_blocks = queries.reshape(CH_DEV, SPAN, cols)
    send_q = query_blocks[send_q_idx]
    recv_q = lax.all_to_all(send_q, ("section", "seq"), split_axis=0, concat_axis=0, tiled=True)

    my_slots = group_index * CAPC + jnp.arange(CAPC, dtype=jnp.int32)
    hit = slot_map[None, :] == my_slots[:, None]
    slot_span = jnp.sum(jnp.where(hit, span_ids[None, :], 0), axis=1)
    slot_group = slot_span // CH_DEV
    slot_place = arrival[slot_span]
    q_for_slot = recv_q[slot_group, slot_place].reshape(CAPC, SPAN, heads_local, HD)

    rows = lax.all_gather(neighbours, "tensor", axis=0, tiled=True)
    rows = rows.reshape(CAPC, KEYS, rows.shape[1])
    kv = jnp.einsum("skd,cde->cske", rows, kv_weight, preferred_element_type=jnp.float32)
    kv = kv.astype(jnp.bfloat16).reshape(2, CAPC, KEYS, heads_local, HD)
    keys, values = kv[0], kv[1]
    attended = attend(q_for_slot, keys, values).reshape(CAPC, SPAN, cols)

    pick_a = (slot_group[None, None, :] == peer_ids) & (slot_place[None, None, :] == place_ids)
    send_a_idx = jnp.sum(
        jnp.where(pick_a, jnp.arange(CAPC, dtype=jnp.int32)[None, None, :], 0), axis=-1
    )
    send_a = attended[send_a_idx]
    recv_a = lax.all_to_all(send_a, ("section", "seq"), split_axis=0, concat_axis=0, tiled=True)
    attended_rows = recv_a[own_owner, own_arrival].reshape(tensor_size, -1, cols)

    partial = jnp.einsum(
        "srk,kn->srn", attended_rows, out_weight, preferred_element_type=jnp.float32
    ).astype(jnp.bfloat16)
    mixed = lax.psum_scatter(partial, "tensor", scatter_dimension=0, tiled=True)
    return mixed.reshape(-1, out_weight.shape[1])


def solution(mesh):
    placed = (
        P(("section", "seq"), "tensor"),
        P(("section", "seq", "tensor"), None),
        P(None, None, "tensor"),
        P("tensor", None),
        P(),
    )
    return jax.shard_map(
        on_device,
        mesh=mesh,
        in_specs=placed,
        out_specs=P(("section", "seq", "tensor"), None),
        check_vma=False,
    )
```

```python
import math

import jax
import jax.numpy as jnp
from jax import lax
from jax.sharding import PartitionSpec as P

HD = 128
SPAN = 64
PEER = 2
CH_DEV = 5
CAPC = 5
KEYS = 256


def attend(query_block, keys, values):
    scores = jnp.einsum(
        "bqhd,bkhd->bhqk", query_block, keys, preferred_element_type=jnp.float32
    )
    scores = scores * (1.0 / math.sqrt(HD))
    peak = jnp.max(scores, axis=-1, keepdims=True)
    expo = jnp.exp(scores - peak)
    weights = (expo / jnp.sum(expo, axis=-1, keepdims=True)).astype(jnp.bfloat16)
    result = jnp.einsum(
        "bhqk,bkhd->bqhd", weights, values, preferred_element_type=jnp.float32
    )
    return result.astype(jnp.bfloat16)


def on_device(queries, neighbours, kv_weight, out_weight, slot_map):
    groups = lax.axis_size(("section", "seq"))
    group_index = lax.axis_index(("section", "seq"))
    tensor_size = lax.axis_size("tensor")
    cols = kv_weight.shape[2]
    heads_local = cols // HD
    spans = slot_map.shape[0]
    rows_local = neighbours.shape[0]

    span_ids = jnp.arange(spans, dtype=jnp.int32)
    owner_shard = slot_map // CAPC
    slot_index = slot_map % CAPC
    seq_owner = span_ids // CH_DEV
    earlier = (seq_owner[:, None] == seq_owner[None, :]) & (
        owner_shard[:, None] == owner_shard[None, :]
    )
    earlier = earlier & (span_ids[None, :] < span_ids[:, None])
    arrival = jnp.sum(earlier.astype(jnp.int32), axis=1)

    peer_ids = jnp.arange(groups, dtype=jnp.int32)[:, None, None]
    place_ids = jnp.arange(PEER, dtype=jnp.int32)[None, :, None]

    own_spans = group_index * CH_DEV + jnp.arange(CH_DEV, dtype=jnp.int32)
    own_owner = owner_shard[own_spans]
    own_arrival = arrival[own_spans]
    pick_q = (own_owner[None, None, :] == peer_ids) & (own_arrival[None, None, :] == place_ids)
    send_q_idx = jnp.sum(
        jnp.where(pick_q, jnp.arange(CH_DEV, dtype=jnp.int32)[None, None, :], 0), axis=-1
    )
    query_blocks = queries.reshape(CH_DEV, SPAN, cols)
    send_q = query_blocks[send_q_idx]
    recv_q = lax.all_to_all(send_q, ("section", "seq"), split_axis=0, concat_axis=0, tiled=True)

    my_slots = group_index * CAPC + jnp.arange(CAPC, dtype=jnp.int32)
    hit = slot_map[None, :] == my_slots[:, None]
    slot_span = jnp.sum(jnp.where(hit, span_ids[None, :], 0), axis=1)
    slot_group = slot_span // CH_DEV
    slot_place = arrival[slot_span]
    q_for_slot = recv_q[slot_group, slot_place].reshape(CAPC, SPAN, heads_local, HD)

    rows = lax.all_gather(neighbours, "tensor", axis=0, tiled=True)
    rows = rows.reshape(CAPC, KEYS, rows.shape[1])
    kv = jnp.einsum("skd,cde->cske", rows, kv_weight, preferred_element_type=jnp.float32)
    kv = kv.astype(jnp.bfloat16).reshape(2, CAPC, KEYS, heads_local, HD)
    keys, values = kv[0], kv[1]
    attended = attend(q_for_slot, keys, values).reshape(CAPC, SPAN, cols)

    pick_a = (slot_group[None, None, :] == peer_ids) & (slot_place[None, None, :] == place_ids)
    send_a_idx = jnp.sum(
        jnp.where(pick_a, jnp.arange(CAPC, dtype=jnp.int32)[None, None, :], 0), axis=-1
    )
    send_a = attended[send_a_idx]
    recv_a = lax.all_to_all(send_a, ("section", "seq"), split_axis=0, concat_axis=0, tiled=True)
    attended_rows = recv_a[own_owner, own_arrival].reshape(tensor_size, -1, cols)

    partial = jnp.einsum(
        "srk,kn->srn", attended_rows, out_weight, preferred_element_type=jnp.float32
    ).astype(jnp.bfloat16)
    pieces = lax.all_to_all(partial, "tensor", split_axis=0, concat_axis=0, tiled=True)
    return jnp.sum(pieces.astype(jnp.float32), axis=0).astype(jnp.bfloat16)


def solution(mesh):
    placed = (
        P(("section", "seq"), "tensor"),
        P(("section", "seq", "tensor"), None),
        P(None, None, "tensor"),
        P("tensor", None),
        P(),
    )
    return jax.shard_map(
        on_device,
        mesh=mesh,
        in_specs=placed,
        out_specs=P(("section", "seq", "tensor"), None),
        check_vma=False,
    )
```

```python
import math

import jax
import jax.numpy as jnp
from jax import lax
from jax.sharding import PartitionSpec as P

HD = 128
SPAN = 64
PEER = 2
CH_DEV = 5
CAPC = 5
KEYS = 256


def attend(query_block, keys, values):
    scores = jnp.einsum(
        "bqhd,bkhd->bhqk", query_block, keys, preferred_element_type=jnp.float32
    )
    scores = scores * (1.0 / math.sqrt(HD))
    peak = jnp.max(scores, axis=-1, keepdims=True)
    expo = jnp.exp(scores - peak)
    weights = (expo / jnp.sum(expo, axis=-1, keepdims=True)).astype(jnp.bfloat16)
    result = jnp.einsum(
        "bhqk,bkhd->bqhd", weights, values, preferred_element_type=jnp.float32
    )
    return result.astype(jnp.bfloat16)


def on_device(queries, neighbours, kv_weight, out_weight, slot_map):
    groups = lax.axis_size(("section", "seq"))
    group_index = lax.axis_index(("section", "seq"))
    tensor_size = lax.axis_size("tensor")
    cols = kv_weight.shape[2]
    heads_local = cols // HD
    spans = slot_map.shape[0]
    rows_local = neighbours.shape[0]

    span_ids = jnp.arange(spans, dtype=jnp.int32)
    owner_shard = slot_map // CAPC
    slot_index = slot_map % CAPC
    seq_owner = span_ids // CH_DEV
    earlier = (seq_owner[:, None] == seq_owner[None, :]) & (
        owner_shard[:, None] == owner_shard[None, :]
    )
    earlier = earlier & (span_ids[None, :] < span_ids[:, None])
    arrival = jnp.sum(earlier.astype(jnp.int32), axis=1)

    peer_ids = jnp.arange(groups, dtype=jnp.int32)[:, None, None]
    place_ids = jnp.arange(PEER, dtype=jnp.int32)[None, :, None]

    own_spans = group_index * CH_DEV + jnp.arange(CH_DEV, dtype=jnp.int32)
    own_owner = owner_shard[own_spans]
    own_arrival = arrival[own_spans]
    pick_q = (own_owner[None, None, :] == peer_ids) & (own_arrival[None, None, :] == place_ids)
    send_q_idx = jnp.sum(
        jnp.where(pick_q, jnp.arange(CH_DEV, dtype=jnp.int32)[None, None, :], 0), axis=-1
    )
    query_blocks = queries.reshape(CH_DEV, SPAN, cols)
    send_q = query_blocks[send_q_idx]
    recv_q = lax.all_to_all(send_q, ("section", "seq"), split_axis=0, concat_axis=0, tiled=True)

    my_slots = group_index * CAPC + jnp.arange(CAPC, dtype=jnp.int32)
    hit = slot_map[None, :] == my_slots[:, None]
    slot_span = jnp.sum(jnp.where(hit, span_ids[None, :], 0), axis=1)
    slot_group = slot_span // CH_DEV
    slot_place = arrival[slot_span]
    q_for_slot = recv_q[slot_group, slot_place].reshape(CAPC, SPAN, heads_local, HD)

    rows = lax.all_gather(neighbours, "tensor", axis=0, tiled=True)
    rows = rows.reshape(CAPC, KEYS, rows.shape[1])
    kv = jnp.einsum("skd,cde->cske", rows, kv_weight, preferred_element_type=jnp.float32)
    kv = kv.astype(jnp.bfloat16).reshape(2, CAPC, KEYS, heads_local, HD)
    keys, values = kv[0], kv[1]
    attended = attend(q_for_slot, keys, values).reshape(CAPC, SPAN, cols)

    pick_a = (slot_group[None, None, :] == peer_ids) & (slot_place[None, None, :] == place_ids)
    send_a_idx = jnp.sum(
        jnp.where(pick_a, jnp.arange(CAPC, dtype=jnp.int32)[None, None, :], 0), axis=-1
    )
    send_a = attended[send_a_idx]
    by_shift = [send_a[group_index]]
    for k in range(1, groups):
        block = lax.dynamic_index_in_dim(send_a, (group_index + k) % groups, 0, keepdims=False)
        pairs = [(s, (s + k) % groups) for s in range(groups)]
        by_shift.append(lax.ppermute(block, ("section", "seq"), pairs))
    recv_a = jnp.stack(by_shift)
    shift_of = (group_index - own_owner) % groups
    attended_rows = recv_a[shift_of, own_arrival].reshape(tensor_size, -1, cols)

    partial = jnp.einsum(
        "srk,kn->srn", attended_rows, out_weight, preferred_element_type=jnp.float32
    ).astype(jnp.bfloat16)
    mixed = lax.psum_scatter(partial, "tensor", scatter_dimension=0, tiled=True)
    return mixed.reshape(-1, out_weight.shape[1])


def solution(mesh):
    placed = (
        P(("section", "seq"), "tensor"),
        P(("section", "seq", "tensor"), None),
        P(None, None, "tensor"),
        P("tensor", None),
        P(),
    )
    return jax.shard_map(
        on_device,
        mesh=mesh,
        in_specs=placed,
        out_specs=P(("section", "seq", "tensor"), None),
        check_vma=False,
    )
```

```python
import math

import jax
import jax.numpy as jnp
from jax import lax
from jax.sharding import PartitionSpec as P

HD = 128
SPAN = 64
PEER = 2
CH_DEV = 5
CAPC = 5
KEYS = 256


def attend(query_block, keys, values):
    scores = jnp.einsum(
        "bqhd,bkhd->bhqk", query_block, keys, preferred_element_type=jnp.float32
    )
    scores = scores * (1.0 / math.sqrt(HD))
    peak = jnp.max(scores, axis=-1, keepdims=True)
    expo = jnp.exp(scores - peak)
    weights = (expo / jnp.sum(expo, axis=-1, keepdims=True)).astype(jnp.bfloat16)
    result = jnp.einsum(
        "bhqk,bkhd->bqhd", weights, values, preferred_element_type=jnp.float32
    )
    return result.astype(jnp.bfloat16)


def on_device(queries, neighbours, kv_weight, out_weight, slot_map):
    groups = lax.axis_size(("section", "seq"))
    group_index = lax.axis_index(("section", "seq"))
    tensor_size = lax.axis_size("tensor")
    cols = kv_weight.shape[2]
    heads_local = cols // HD
    spans = slot_map.shape[0]
    rows_local = neighbours.shape[0]

    span_ids = jnp.arange(spans, dtype=jnp.int32)
    owner_shard = slot_map // CAPC
    slot_index = slot_map % CAPC
    seq_owner = span_ids // CH_DEV
    earlier = (seq_owner[:, None] == seq_owner[None, :]) & (
        owner_shard[:, None] == owner_shard[None, :]
    )
    earlier = earlier & (span_ids[None, :] < span_ids[:, None])
    arrival = jnp.sum(earlier.astype(jnp.int32), axis=1)

    peer_ids = jnp.arange(groups, dtype=jnp.int32)[:, None, None]
    place_ids = jnp.arange(PEER, dtype=jnp.int32)[None, :, None]

    own_spans = group_index * CH_DEV + jnp.arange(CH_DEV, dtype=jnp.int32)
    own_owner = owner_shard[own_spans]
    own_arrival = arrival[own_spans]
    pick_q = (own_owner[None, None, :] == peer_ids) & (own_arrival[None, None, :] == place_ids)
    send_q_idx = jnp.sum(
        jnp.where(pick_q, jnp.arange(CH_DEV, dtype=jnp.int32)[None, None, :], 0), axis=-1
    )
    query_blocks = queries.reshape(CH_DEV, SPAN, cols)
    send_q = query_blocks[send_q_idx]
    recv_q = lax.all_to_all(send_q, ("section", "seq"), split_axis=0, concat_axis=0, tiled=True)

    my_slots = group_index * CAPC + jnp.arange(CAPC, dtype=jnp.int32)
    hit = slot_map[None, :] == my_slots[:, None]
    slot_span = jnp.sum(jnp.where(hit, span_ids[None, :], 0), axis=1)
    slot_group = slot_span // CH_DEV
    slot_place = arrival[slot_span]
    q_for_slot = recv_q[slot_group, slot_place].reshape(CAPC, SPAN, heads_local, HD)

    rows = lax.all_gather(neighbours, "tensor", axis=0, tiled=True)
    rows = rows.reshape(CAPC, KEYS, rows.shape[1])
    kv = jnp.einsum("skd,cde->cske", rows, kv_weight, preferred_element_type=jnp.float32)
    kv = kv.astype(jnp.bfloat16).reshape(2, CAPC, KEYS, heads_local, HD)
    keys, values = kv[0], kv[1]
    attended = attend(q_for_slot, keys, values).reshape(CAPC, SPAN, cols)

    pick_a = (slot_group[None, None, :] == peer_ids) & (slot_place[None, None, :] == place_ids)
    send_a_idx = jnp.sum(
        jnp.where(pick_a, jnp.arange(CAPC, dtype=jnp.int32)[None, None, :], 0), axis=-1
    )
    send_a = attended[send_a_idx]
    by_shift = [send_a[group_index]]
    for k in range(1, groups):
        block = lax.dynamic_index_in_dim(send_a, (group_index + k) % groups, 0, keepdims=False)
        pairs = [(s, (s + k) % groups) for s in range(groups)]
        by_shift.append(lax.ppermute(block, ("section", "seq"), pairs))
    recv_a = jnp.stack(by_shift)
    shift_of = (group_index - own_owner) % groups
    attended_rows = recv_a[shift_of, own_arrival].reshape(tensor_size, -1, cols)

    half = out_weight.shape[1] // 2
    partial_a = jnp.einsum(
        "srk,kn->srn", attended_rows, out_weight[:, :half], preferred_element_type=jnp.float32
    ).astype(jnp.bfloat16)
    mixed_a = lax.psum_scatter(partial_a, "tensor", scatter_dimension=0, tiled=True)[0]
    partial_b = jnp.einsum(
        "srk,kn->srn", attended_rows, out_weight[:, half:], preferred_element_type=jnp.float32
    ).astype(jnp.bfloat16)
    pieces = lax.all_to_all(partial_b, "tensor", split_axis=0, concat_axis=0, tiled=True)
    mixed_b = jnp.sum(pieces.astype(jnp.float32), axis=0).astype(jnp.bfloat16)
    return jnp.concatenate([mixed_a, mixed_b], axis=1)

def solution(mesh):
    placed = (
        P(("section", "seq"), "tensor"),
        P(("section", "seq", "tensor"), None),
        P(None, None, "tensor"),
        P("tensor", None),
        P(),
    )
    return jax.shard_map(
        on_device,
        mesh=mesh,
        in_specs=placed,
        out_specs=P(("section", "seq", "tensor"), None),
        check_vma=False,
    )
```

```python
import math

import jax
import jax.numpy as jnp
from jax import lax
from jax.sharding import PartitionSpec as P

HD = 128
SPAN = 64
PEER = 2
CH_DEV = 5
CAPC = 5
KEYS = 256


def attend(query_block, keys, values):
    scores = jnp.einsum(
        "bqhd,bkhd->bhqk", query_block, keys, preferred_element_type=jnp.float32
    )
    scores = scores * (1.0 / math.sqrt(HD))
    peak = jnp.max(scores, axis=-1, keepdims=True)
    expo = jnp.exp(scores - peak)
    weights = (expo / jnp.sum(expo, axis=-1, keepdims=True)).astype(jnp.bfloat16)
    result = jnp.einsum(
        "bhqk,bkhd->bqhd", weights, values, preferred_element_type=jnp.float32
    )
    return result.astype(jnp.bfloat16)


def on_device(queries, neighbours, kv_weight, out_weight, slot_map):
    groups = lax.axis_size(("section", "seq"))
    group_index = lax.axis_index(("section", "seq"))
    tensor_size = lax.axis_size("tensor")
    cols = kv_weight.shape[2]
    heads_local = cols // HD
    spans = slot_map.shape[0]
    rows_local = neighbours.shape[0]

    span_ids = jnp.arange(spans, dtype=jnp.int32)
    owner_shard = slot_map // CAPC
    slot_index = slot_map % CAPC
    seq_owner = span_ids // CH_DEV
    earlier = (seq_owner[:, None] == seq_owner[None, :]) & (
        owner_shard[:, None] == owner_shard[None, :]
    )
    earlier = earlier & (span_ids[None, :] < span_ids[:, None])
    arrival = jnp.sum(earlier.astype(jnp.int32), axis=1)

    peer_ids = jnp.arange(groups, dtype=jnp.int32)[:, None, None]
    place_ids = jnp.arange(PEER, dtype=jnp.int32)[None, :, None]

    own_spans = group_index * CH_DEV + jnp.arange(CH_DEV, dtype=jnp.int32)
    own_owner = owner_shard[own_spans]
    own_arrival = arrival[own_spans]
    pick_q = (own_owner[None, None, :] == peer_ids) & (own_arrival[None, None, :] == place_ids)
    send_q_idx = jnp.sum(
        jnp.where(pick_q, jnp.arange(CH_DEV, dtype=jnp.int32)[None, None, :], 0), axis=-1
    )
    query_blocks = queries.reshape(CH_DEV, SPAN, cols)
    send_q = query_blocks[send_q_idx]
    recv_q = lax.all_to_all(send_q, ("section", "seq"), split_axis=0, concat_axis=0, tiled=True)

    my_slots = group_index * CAPC + jnp.arange(CAPC, dtype=jnp.int32)
    hit = slot_map[None, :] == my_slots[:, None]
    slot_span = jnp.sum(jnp.where(hit, span_ids[None, :], 0), axis=1)
    slot_group = slot_span // CH_DEV
    slot_place = arrival[slot_span]
    q_for_slot = recv_q[slot_group, slot_place].reshape(CAPC, SPAN, heads_local, HD)

    rows = lax.all_gather(neighbours, "tensor", axis=0, tiled=True)
    rows = rows.reshape(CAPC, KEYS, rows.shape[1])
    kv = jnp.einsum("skd,cde->cske", rows, kv_weight, preferred_element_type=jnp.float32)
    kv = kv.astype(jnp.bfloat16).reshape(2, CAPC, KEYS, heads_local, HD)
    keys, values = kv[0], kv[1]
    attended = attend(q_for_slot, keys, values).reshape(CAPC, SPAN, cols)

    pick_a = (slot_group[None, None, :] == peer_ids) & (slot_place[None, None, :] == place_ids)
    send_a_idx = jnp.sum(
        jnp.where(pick_a, jnp.arange(CAPC, dtype=jnp.int32)[None, None, :], 0), axis=-1
    )
    by_shift = [attended[send_a_idx[group_index]]]
    for k in range(1, groups):
        block = attended[send_a_idx[(group_index + k) % groups]]
        pairs = [(s, (s + k) % groups) for s in range(groups)]
        by_shift.append(lax.ppermute(block, ("section", "seq"), pairs))
    recv_a = jnp.stack(by_shift)
    shift_of = (group_index - own_owner) % groups
    attended_rows = recv_a[shift_of, own_arrival].reshape(tensor_size, -1, cols)

    partial = jnp.einsum(
        "srk,kn->srn", attended_rows, out_weight, preferred_element_type=jnp.float32
    ).astype(jnp.bfloat16)
    mixed = lax.psum_scatter(partial, "tensor", scatter_dimension=0, tiled=True)
    return mixed.reshape(-1, out_weight.shape[1])


def solution(mesh):
    placed = (
        P(("section", "seq"), "tensor"),
        P(("section", "seq", "tensor"), None),
        P(None, None, "tensor"),
        P("tensor", None),
        P(),
    )
    return jax.shard_map(
        on_device,
        mesh=mesh,
        in_specs=placed,
        out_specs=P(("section", "seq", "tensor"), None),
        check_vma=False,
    )
```

```python
import math

import jax
import jax.numpy as jnp
from jax import lax
from jax.sharding import PartitionSpec as P

HD = 128
SPAN = 64
PEER = 2
CH_DEV = 5
CAPC = 5
KEYS = 256


def attend(query_block, keys, values):
    scores = jnp.einsum(
        "bqhd,bkhd->bhqk", query_block, keys, preferred_element_type=jnp.float32
    )
    scores = scores * (1.0 / math.sqrt(HD))
    peak = jnp.max(scores, axis=-1, keepdims=True)
    expo = jnp.exp(scores - peak)
    weights = (expo / jnp.sum(expo, axis=-1, keepdims=True)).astype(jnp.bfloat16)
    result = jnp.einsum(
        "bhqk,bkhd->bhqd", weights, values, preferred_element_type=jnp.float32
    )
    return result.astype(jnp.bfloat16)


def on_device(queries, neighbours, kv_weight, out_weight, slot_map):
    groups = lax.axis_size(("section", "seq"))
    group_index = lax.axis_index(("section", "seq"))
    tensor_size = lax.axis_size("tensor")
    cols = kv_weight.shape[2]
    heads_local = cols // HD
    spans = slot_map.shape[0]
    rows_local = neighbours.shape[0]

    span_ids = jnp.arange(spans, dtype=jnp.int32)
    owner_shard = slot_map // CAPC
    slot_index = slot_map % CAPC
    seq_owner = span_ids // CH_DEV
    earlier = (seq_owner[:, None] == seq_owner[None, :]) & (
        owner_shard[:, None] == owner_shard[None, :]
    )
    earlier = earlier & (span_ids[None, :] < span_ids[:, None])
    arrival = jnp.sum(earlier.astype(jnp.int32), axis=1)

    peer_ids = jnp.arange(groups, dtype=jnp.int32)[:, None, None]
    place_ids = jnp.arange(PEER, dtype=jnp.int32)[None, :, None]

    own_spans = group_index * CH_DEV + jnp.arange(CH_DEV, dtype=jnp.int32)
    own_owner = owner_shard[own_spans]
    own_arrival = arrival[own_spans]
    pick_q = (own_owner[None, None, :] == peer_ids) & (own_arrival[None, None, :] == place_ids)
    send_q_idx = jnp.sum(
        jnp.where(pick_q, jnp.arange(CH_DEV, dtype=jnp.int32)[None, None, :], 0), axis=-1
    )
    query_blocks = queries.reshape(CH_DEV, SPAN, cols)
    send_q = query_blocks[send_q_idx]
    recv_q = lax.all_to_all(send_q, ("section", "seq"), split_axis=0, concat_axis=0, tiled=True)

    my_slots = group_index * CAPC + jnp.arange(CAPC, dtype=jnp.int32)
    hit = slot_map[None, :] == my_slots[:, None]
    slot_span = jnp.sum(jnp.where(hit, span_ids[None, :], 0), axis=1)
    slot_group = slot_span // CH_DEV
    slot_place = arrival[slot_span]
    q_for_slot = recv_q[slot_group, slot_place].reshape(CAPC, SPAN, heads_local, HD)

    rows = lax.all_gather(neighbours, "tensor", axis=0, tiled=True)
    rows = rows.reshape(CAPC, KEYS, rows.shape[1])
    kv = jnp.einsum("skd,cde->cske", rows, kv_weight, preferred_element_type=jnp.float32)
    kv = kv.astype(jnp.bfloat16).reshape(2, CAPC, KEYS, heads_local, HD)
    keys, values = kv[0], kv[1]
    attended = attend(q_for_slot, keys, values)

    pick_a = (slot_group[None, None, :] == peer_ids) & (slot_place[None, None, :] == place_ids)
    send_a_idx = jnp.sum(
        jnp.where(pick_a, jnp.arange(CAPC, dtype=jnp.int32)[None, None, :], 0), axis=-1
    )
    send_a = attended[send_a_idx]
    by_shift = [send_a[group_index]]
    for k in range(1, groups):
        block = lax.dynamic_index_in_dim(send_a, (group_index + k) % groups, 0, keepdims=False)
        pairs = [(s, (s + k) % groups) for s in range(groups)]
        by_shift.append(lax.ppermute(block, ("section", "seq"), pairs))
    recv_a = jnp.stack(by_shift)
    shift_of = (group_index - own_owner) % groups
    attended_rows = jnp.swapaxes(recv_a[shift_of, own_arrival], 1, 2)
    attended_rows = attended_rows.reshape(tensor_size, -1, cols)

    partial = jnp.einsum(
        "srk,kn->srn", attended_rows, out_weight, preferred_element_type=jnp.float32
    ).astype(jnp.bfloat16)
    mixed = lax.psum_scatter(partial, "tensor", scatter_dimension=0, tiled=True)
    return mixed.reshape(-1, out_weight.shape[1])


def solution(mesh):
    placed = (
        P(("section", "seq"), "tensor"),
        P(("section", "seq", "tensor"), None),
        P(None, None, "tensor"),
        P("tensor", None),
        P(),
    )
    return jax.shard_map(
        on_device,
        mesh=mesh,
        in_specs=placed,
        out_specs=P(("section", "seq", "tensor"), None),
        check_vma=False,
    )
```

```python
import math

import jax
import jax.numpy as jnp
from jax import lax
from jax.sharding import PartitionSpec as P

HD = 128
SPAN = 64
PEER = 2
CH_DEV = 5
CAPC = 5
KEYS = 256


def attend(query_block, keys, values):
    scores = jnp.einsum(
        "bqhd,bkhd->bhqk", query_block, keys, preferred_element_type=jnp.float32
    )
    scores = scores * (1.0 / math.sqrt(HD))
    peak = jnp.max(scores, axis=-1, keepdims=True)
    expo = jnp.exp(scores - peak)
    weights = (expo / jnp.sum(expo, axis=-1, keepdims=True)).astype(jnp.bfloat16)
    result = jnp.einsum(
        "bhqk,bkhd->bqhd", weights, values, preferred_element_type=jnp.float32
    )
    return result.astype(jnp.bfloat16)


def on_device(queries, neighbours, kv_weight, out_weight, slot_map):
    groups = lax.axis_size(("section", "seq"))
    group_index = lax.axis_index(("section", "seq"))
    tensor_size = lax.axis_size("tensor")
    cols = kv_weight.shape[2]
    heads_local = cols // HD
    spans = slot_map.shape[0]
    rows_local = neighbours.shape[0]

    span_ids = jnp.arange(spans, dtype=jnp.int32)
    owner_shard = slot_map // CAPC
    slot_index = slot_map % CAPC
    seq_owner = span_ids // CH_DEV
    earlier = (seq_owner[:, None] == seq_owner[None, :]) & (
        owner_shard[:, None] == owner_shard[None, :]
    )
    earlier = earlier & (span_ids[None, :] < span_ids[:, None])
    arrival = jnp.sum(earlier.astype(jnp.int32), axis=1)

    peer_ids = jnp.arange(groups, dtype=jnp.int32)[:, None, None]
    place_ids = jnp.arange(PEER, dtype=jnp.int32)[None, :, None]

    own_spans = group_index * CH_DEV + jnp.arange(CH_DEV, dtype=jnp.int32)
    own_owner = owner_shard[own_spans]
    own_arrival = arrival[own_spans]
    pick_q = (own_owner[None, None, :] == peer_ids) & (own_arrival[None, None, :] == place_ids)
    send_q_idx = jnp.sum(
        jnp.where(pick_q, jnp.arange(CH_DEV, dtype=jnp.int32)[None, None, :], 0), axis=-1
    )
    query_blocks = queries.reshape(CH_DEV, SPAN, cols)
    send_q = query_blocks[send_q_idx]
    q_by_shift = [send_q[group_index]]
    for k in range(1, groups):
        block = lax.dynamic_index_in_dim(send_q, (group_index + k) % groups, 0, keepdims=False)
        pairs = [(s, (s + k) % groups) for s in range(groups)]
        q_by_shift.append(lax.ppermute(block, ("section", "seq"), pairs))
    recv_q = jnp.stack(q_by_shift)

    my_slots = group_index * CAPC + jnp.arange(CAPC, dtype=jnp.int32)
    hit = slot_map[None, :] == my_slots[:, None]
    slot_span = jnp.sum(jnp.where(hit, span_ids[None, :], 0), axis=1)
    slot_group = slot_span // CH_DEV
    slot_place = arrival[slot_span]
    q_for_slot = recv_q[(group_index - slot_group) % groups, slot_place]
    q_for_slot = q_for_slot.reshape(CAPC, SPAN, heads_local, HD)

    rows = lax.all_gather(neighbours, "tensor", axis=0, tiled=True)
    rows = rows.reshape(CAPC, KEYS, rows.shape[1])
    kv = jnp.einsum("skd,cde->cske", rows, kv_weight, preferred_element_type=jnp.float32)
    kv = kv.astype(jnp.bfloat16).reshape(2, CAPC, KEYS, heads_local, HD)
    keys, values = kv[0], kv[1]
    attended = attend(q_for_slot, keys, values).reshape(CAPC, SPAN, cols)

    pick_a = (slot_group[None, None, :] == peer_ids) & (slot_place[None, None, :] == place_ids)
    send_a_idx = jnp.sum(
        jnp.where(pick_a, jnp.arange(CAPC, dtype=jnp.int32)[None, None, :], 0), axis=-1
    )
    send_a = attended[send_a_idx]
    by_shift = [send_a[group_index]]
    for k in range(1, groups):
        block = lax.dynamic_index_in_dim(send_a, (group_index + k) % groups, 0, keepdims=False)
        pairs = [(s, (s + k) % groups) for s in range(groups)]
        by_shift.append(lax.ppermute(block, ("section", "seq"), pairs))
    recv_a = jnp.stack(by_shift)
    shift_of = (group_index - own_owner) % groups
    attended_rows = recv_a[shift_of, own_arrival].reshape(tensor_size, -1, cols)

    partial = jnp.einsum(
        "srk,kn->srn", attended_rows, out_weight, preferred_element_type=jnp.float32
    ).astype(jnp.bfloat16)
    mixed = lax.psum_scatter(partial, "tensor", scatter_dimension=0, tiled=True)
    return mixed.reshape(-1, out_weight.shape[1])


def solution(mesh):
    placed = (
        P(("section", "seq"), "tensor"),
        P(("section", "seq", "tensor"), None),
        P(None, None, "tensor"),
        P("tensor", None),
        P(),
    )
    return jax.shard_map(
        on_device,
        mesh=mesh,
        in_specs=placed,
        out_specs=P(("section", "seq", "tensor"), None),
        check_vma=False,
    )
```
